128 devices in a mesh: req: 32 (over z, x, core), mlp: 4 (over y).
Axes of the slice: x: 4, y: 4, z: 4, core: 2. Of those that a mesh axis runs over, the one named last changes fastest.
Arguments:
- patches: bfloat16 [8192, 4, 1664], P('req', 'mlp'), may hold values from -6 to 6
- vis_gain: float32 [1664], replicated, may hold values from 0.1 to 1.9
- vis_proj: bfloat16 [6656, 1664], P('mlp'), may hold values from -0.078125 to 0.078125
- targets: int32 [8192], P('req'), may hold values from 0 to 32767, as said below
- lengths: int32 [32], P('req'), may hold values from 512 to 1024, as said below
- text: bfloat16 [32768, 1664], P('req'), may hold values from -6 to 6
- attn_gain: float32 [1664], replicated, may hold values from 0.1 to 1.9
- wqkv: bfloat16 [1664, 4992], P(None, 'mlp'), as said below
- wo: bfloat16 [1664, 1664], P('mlp'), may hold values from -0.15625 to 0.15625
- mlp_gain: float32 [1664], replicated, may hold values from 0.1 to 1.9
- w_in: bfloat16 [1664, 8192], P('req', 'mlp'), may hold values from -0.15625 to 0.15625
- w_out: bfloat16 [8192, 1664], P('mlp', 'req'), may hold values from -0.0625 to 0.0625
Outputs:
- layer_out: bfloat16 [32768, 1664], P(('req', 'mlp'))
The draws below stay inside these ranges and needn't reach their ends.
Inputs may be any that keep to these rules, and one draw needn't show every extreme that they name: targets[m] = 1024 * prompt + slot, all distinct, every slot below its prompt's length. The rows of one vision device go to one prompt 16 times at most, and this is reached in every draw. `lengths`: some prompt has length 1024. `wqkv`: projection weights, each within -1.8 to 1.8; a head's query and key columns may be much larger than its value columns.
All inputs are finite; a program needn't handle non-finite values.
Results may differ from the reference program's by a relative error of at most 0.027.
The reference program's roundings to bfloat16 on the way count: a program that leaves them out, or rounds other values in their place, can miss the bound.
Values may be sent and summed in bfloat16 or wider, within the bound.
No kernel may reach another device: no remote copies, remote signals or barrier semaphores. Data moves between devices by JAX's collectives and lax.ppermute only.
A program may use at most 128 MiB of HBM per device.

```python
import jax
import jax.numpy as jnp
from jax import lax

D = 1664
HEADS = 16
HD = 104
FF = 8192
SEQ = 1024
MERGED = 256
REQS = 32
CAP = 16
SLOTS = 8192
N_MLP = 4


def shared_plan(key):
    base = jax.random.fold_in(key, 11)
    key_len, key_forced, key_lift, key_perm, key_order, key_shuffle = jax.random.split(base, 6)
    prompt_ids = jnp.arange(REQS)
    prompt_len = jax.random.randint(key_len, (REQS,), 2 * MERGED, SEQ + 1)
    forced = jax.random.randint(key_forced, (), 0, REQS)
    prompt_len = jnp.where(prompt_ids == forced, SEQ, prompt_len).astype(jnp.int32)
    half_cap = CAP // 2
    lifted = jax.random.randint(key_lift, (REQS, REQS // 2), 0, half_cap + 1)
    lifted = lifted.at[:, 0].set(half_cap)
    loads = jnp.stack([half_cap + lifted, half_cap - lifted], axis=-1).reshape(REQS, REQS)
    orders_dest = jax.vmap(lambda sub_key: jax.random.permutation(sub_key, REQS))(jax.random.split(key_perm, REQS))
    counts = jnp.zeros((REQS, REQS), jnp.int32).at[prompt_ids[:, None], orders_dest].set(loads.astype(jnp.int32))
    earlier = jnp.cumsum(counts, axis=0) - counts
    slot_orders = jax.vmap(lambda sub_key: jax.random.permutation(sub_key, SEQ))(jax.random.split(key_order, REQS))
    outside = (slot_orders >= prompt_len[:, None]).astype(jnp.int32)
    ranking = jnp.argsort(outside, axis=1, stable=True)
    free_slots = jnp.take_along_axis(slot_orders, ranking, axis=1)

    def one_source(counts_row, offsets, sub_key):
        ends = jnp.cumsum(counts_row)
        slot_ids = jnp.arange(MERGED)
        target_req = jnp.sum((ends[None, :] <= slot_ids[:, None]).astype(jnp.int32), axis=1)
        inner = slot_ids - (ends[target_req] - counts_row[target_req])
        position = free_slots[target_req, offsets[target_req] + inner]
        flat_index = target_req * SEQ + position
        return flat_index[jax.random.permutation(sub_key, MERGED)]
    flat_all = jax.vmap(one_source)(counts, earlier, jax.random.split(key_shuffle, REQS))
    return (flat_all.reshape(-1).astype(jnp.int32), prompt_len)


def draw_targets(key, part):
    return shared_plan(key)[0]


def draw_lengths(key, part):
    return shared_plan(key)[1]


def draw_wqkv(key, part):
    values = jax.random.normal(key, (D, HEADS * 3 * HD), jnp.float32)
    values = jnp.clip(values, -6.0, 6.0) / jnp.float32(D) ** 0.5
    return values.astype(jnp.bfloat16)


def levels(stream_key, extent, pieces, low, top_value):
    level, own = 1.0, jax.random.fold_in(stream_key, 6)
    for axis_at, blocks in pieces:
        heights = jnp.exp(jax.random.uniform(jax.random.fold_in(own, axis_at), (blocks,), jnp.float32, low / len(pieces), top_value / len(pieces)))
        level = level * jnp.repeat(heights, extent[axis_at] // blocks).reshape([-1 if axis == axis_at else 1 for axis in range(len(extent))])
    return level


def bell_draw(stream_key, shape, deviation, limit, pieces=(), dtype=jnp.bfloat16):
    loudness = levels(stream_key, shape, pieces, -0.22, 0.18) if pieces else 1.0
    array = jax.random.normal(stream_key, shape, jnp.float32) * deviation * loudness
    return jnp.minimum(jnp.maximum(array, -limit), limit).astype(dtype)


def setup_inputs(seed: int = 0) -> dict:
    streams_of = jax.random.split(jax.random.key(seed), 13)
    return {
        "patches": bell_draw(streams_of[0], (SLOTS, 4, D), 1.0, 6.0, ((0, 32), (1, 4))),
        "vis_gain": jnp.clip(1.0 + 0.18 * jax.random.normal(streams_of[1], (D,), jnp.float32), 0.1, 1.9),
        "vis_proj": bell_draw(streams_of[2], (4 * D, D), (4 * D) ** -0.5, 0.078125, ((0, 4),)),
        "targets": draw_targets(jax.random.fold_in(streams_of[12], 71), 0),
        "lengths": draw_lengths(jax.random.fold_in(streams_of[12], 71), 0),
        "text": bell_draw(streams_of[5], (REQS * SEQ, D), 1.0, 6.0, ((0, 32),)),
        "attn_gain": jnp.clip(1.0 + 0.18 * jax.random.normal(streams_of[6], (D,), jnp.float32), 0.1, 1.9),
        "wqkv": draw_wqkv(jax.random.fold_in(streams_of[12], 71), 0),
        "wo": bell_draw(streams_of[8], (HEADS * HD, D), (HEADS * HD) ** -0.5, 0.15625, ((0, 4),)),
        "mlp_gain": jnp.clip(1.0 + 0.18 * jax.random.normal(streams_of[9], (D,), jnp.float32), 0.1, 1.9),
        "w_in": bell_draw(streams_of[10], (D, FF), D ** -0.5, 0.15625, ((0, 32), (1, 4))),
        "w_out": bell_draw(streams_of[11], (FF, D), FF ** -0.5, 0.0625, ((0, 4), (1, 32))),
    }


def rms_scale(values, gain):
    wide = values.astype(jnp.float32)
    power = lax.optimization_barrier(jnp.mean(wide * wide, axis=-1, keepdims=True))
    return wide * lax.rsqrt(power + 1e-06) * gain

def per_prompt(item, wqkv, wo, attn_gain, mlp_gain, w_in, w_out):
    embedded, length = item
    attn_in = rms_scale(embedded, attn_gain).astype(jnp.bfloat16)
    qkv = jnp.dot(attn_in, wqkv, preferred_element_type=jnp.float32).astype(jnp.bfloat16)
    qkv = qkv.reshape(SEQ, HEADS, 3, HD).astype(jnp.float32)
    query, keys, values = (qkv[:, :, 0], qkv[:, :, 1], qkv[:, :, 2])
    scores = jnp.einsum('qhd,khd->hqk', query, keys) / jnp.float32(HD) ** 0.5
    row_ids = jnp.arange(SEQ)
    causal = row_ids[None, :] <= row_ids[:, None]
    scores = jnp.where(causal[None], scores, jnp.float32(-1e+30))
    peak = lax.optimization_barrier(jnp.max(scores, axis=-1, keepdims=True))
    weights = jnp.exp(scores - peak)
    probs = (weights / lax.optimization_barrier(jnp.sum(weights, axis=-1, keepdims=True))).astype(jnp.bfloat16)
    context = jnp.einsum('hqk,khd->qhd', probs.astype(jnp.float32), values).astype(jnp.bfloat16)
    context = context.reshape(SEQ, HEADS * HD)
    group_cols = HEADS * HD // N_MLP
    attn_total = jnp.zeros((SEQ, D), jnp.float32)
    for group in range(N_MLP):
        piece = jnp.dot(context[:, group * group_cols:(group + 1) * group_cols], wo[group * group_cols:(group + 1) * group_cols], preferred_element_type=jnp.float32)
        attn_total = attn_total + lax.optimization_barrier(piece.astype(jnp.bfloat16)).astype(jnp.float32)
    resid = embedded.astype(jnp.float32) + attn_total
    mlp_in = rms_scale(resid, mlp_gain).astype(jnp.bfloat16)
    hidden_cols = FF // N_MLP
    mlp_total = jnp.zeros((SEQ, D), jnp.float32)
    for group in range(N_MLP):
        upward = jnp.dot(mlp_in, w_in[:, group * hidden_cols:(group + 1) * hidden_cols], preferred_element_type=jnp.float32)
        active = jax.nn.gelu(upward, approximate=False).astype(jnp.bfloat16)
        piece = jnp.dot(active, w_out[group * hidden_cols:(group + 1) * hidden_cols], preferred_element_type=jnp.float32)
        mlp_total = mlp_total + lax.optimization_barrier(piece.astype(jnp.bfloat16)).astype(jnp.float32)
    result = resid + mlp_total
    valid = row_ids < length
    return jnp.where(valid[:, None], result, jnp.float32(0.0)).astype(jnp.bfloat16)

def reference(patches, vis_gain, vis_proj, targets, lengths, text, attn_gain, wqkv, wo, mlp_gain, w_in, w_out):
    patch_norm = rms_scale(patches, vis_gain).astype(jnp.bfloat16)
    merged_rows = patch_norm.reshape(patches.shape[0], 4 * D)
    image_rows = jnp.dot(merged_rows, vis_proj, preferred_element_type=jnp.float32).astype(jnp.bfloat16)
    embedded = text.at[targets].set(image_rows)
    prompts = embedded.reshape(REQS, SEQ, D)

    def apply_one(item):
        return per_prompt(item, wqkv, wo, attn_gain, mlp_gain, w_in, w_out)
    result = lax.map(apply_one, (prompts, lengths))
    return result.reshape(REQS * SEQ, D)
```

```python
import jax
import jax.numpy as jnp
from jax import lax
from jax.sharding import PartitionSpec as P

HD = 104


def rms_scale(values, gain):
    wide = values.astype(jnp.float32)
    power = jnp.mean(wide * wide, axis=-1, keepdims=True)
    return wide * lax.rsqrt(power + 1e-06) * gain


def shards(
    patches, vis_gain, vis_proj, targets, lengths, text, attn_gain, wqkv, wo, mlp_gain, w_in, w_out
):
    requests = lax.axis_size("req")
    seq_len = text.shape[0]
    width = text.shape[1]
    merged_count = patches.shape[0]
    capacity = 2 * merged_count // requests
    patch_norm = rms_scale(patches[:, 0, :], vis_gain).astype(jnp.bfloat16)
    partial_value = jnp.dot(patch_norm, vis_proj, preferred_element_type=jnp.float32)
    target_req = targets // seq_len
    position = targets % seq_len
    one_hot = (target_req[:, None] == jnp.arange(requests)[None, :]).astype(jnp.int32)
    before = jnp.cumsum(one_hot, axis=0) - one_hot
    rank_in = jnp.sum(before * one_hot, axis=1)
    slot_ids = target_req * capacity + rank_in
    slot_fill = jnp.full((requests * capacity,), -1, jnp.int32).at[slot_ids].set(position)
    slot_fill = slot_fill.reshape(requests, capacity)
    n_mlp = lax.axis_size("mlp")
    group = lax.axis_index("mlp")
    vis_pieces = lax.all_to_all(
        partial_value.reshape(n_mlp, merged_count // n_mlp, width), "mlp", 0, 0, tiled=True
    )
    vis_mine = jnp.sum(vis_pieces, axis=0).astype(jnp.bfloat16)
    image_rows = lax.all_to_all(
        jnp.broadcast_to(vis_mine[None], (n_mlp,) + vis_mine.shape), "mlp", 0, 0, tiled=True
    ).reshape(merged_count, width)
    buffer = jnp.zeros((requests * capacity, width), jnp.bfloat16).at[slot_ids].set(image_rows)
    buffer = buffer.reshape(requests, capacity, width)
    received, got_slots = (
        lax.all_to_all(buffer, "req", split_axis=0, concat_axis=0, tiled=True),
        lax.all_to_all(slot_fill, "req", split_axis=0, concat_axis=0, tiled=True),
    )
    arrived = received.reshape(requests * capacity, width)
    flat_slots = got_slots.reshape(-1)
    flat_slots = jnp.where(flat_slots < 0, seq_len, flat_slots)
    embedded = text.at[flat_slots].set(arrived, mode="drop")
    attn_in = rms_scale(embedded, attn_gain).astype(jnp.bfloat16)
    qkv = jnp.dot(attn_in, wqkv, preferred_element_type=jnp.float32).astype(jnp.bfloat16)
    local_heads = wqkv.shape[1] // (3 * HD)
    qkv = qkv.reshape(seq_len, local_heads, 3, HD)
    query, keys, values = (qkv[:, :, 0], qkv[:, :, 1], qkv[:, :, 2])
    scores = (
        jnp.einsum("qhd,khd->hqk", query, keys, preferred_element_type=jnp.float32)
        / jnp.float32(HD) ** 0.5
    )
    row_ids = jnp.arange(seq_len)
    causal = row_ids[None, :] <= row_ids[:, None]
    scores = jnp.where(causal[None], scores, jnp.float32(-1e30))
    peak = jnp.max(scores, axis=-1, keepdims=True)
    weights = jnp.exp(scores - peak)
    probs = (weights / jnp.sum(weights, axis=-1, keepdims=True)).astype(jnp.bfloat16)
    context = jnp.einsum("hqk,khd->qhd", probs, values, preferred_element_type=jnp.float32).astype(
        jnp.bfloat16
    )
    context = context.reshape(seq_len, local_heads * HD)
    attn_part = jnp.dot(context, wo, preferred_element_type=jnp.float32).astype(jnp.bfloat16)
    share_rows = seq_len // n_mlp
    share_start = group * share_rows
    attn_pieces = lax.all_to_all(
        attn_part.reshape(n_mlp, share_rows, width), "mlp", 0, 0, tiled=True
    ).astype(jnp.float32)
    embedded_share = lax.dynamic_slice_in_dim(embedded, share_start, share_rows, 0)
    resid_share = embedded_share.astype(jnp.float32) + jnp.sum(attn_pieces, axis=0)
    mlp_in_share = rms_scale(resid_share, mlp_gain).astype(jnp.bfloat16)
    mlp_in = lax.all_to_all(
        jnp.broadcast_to(mlp_in_share[None], (n_mlp,) + mlp_in_share.shape), "mlp", 0, 0, tiled=True
    ).reshape(seq_len, width)
    blocks = lax.all_gather(jnp.concatenate([w_in, w_out.T], axis=0), "req", axis=0)
    in_rows = w_in.shape[0]
    w_in_full = blocks[:, :in_rows].reshape(-1, w_in.shape[1])
    w_out_t = blocks[:, in_rows:].reshape(-1, w_in.shape[1])
    upward = jnp.dot(mlp_in, w_in_full, preferred_element_type=jnp.float32)
    active = jax.nn.gelu(upward, approximate=False).astype(jnp.bfloat16)
    mlp_part = lax.dot_general(
        active, w_out_t, (((1,), (1,)), ((), ())), preferred_element_type=jnp.float32
    ).astype(jnp.bfloat16)
    mlp_pieces = lax.all_to_all(
        mlp_part.reshape(n_mlp, share_rows, width), "mlp", 0, 0, tiled=True
    ).astype(jnp.float32)
    result = resid_share + jnp.sum(mlp_pieces, axis=0)
    share_ids = share_start + jnp.arange(share_rows)
    valid = share_ids < lengths[0]
    return jnp.where(valid[:, None], result, jnp.float32(0.0)).astype(jnp.bfloat16)


def solution(mesh):
    return jax.shard_map(
        shards,
        mesh=mesh,
        in_specs=(
            P("req", "mlp", None),
            P(),
            P("mlp", None),
            P("req"),
            P("req"),
            P("req", None),
            P(),
            P(None, "mlp"),
            P("mlp", None),
            P(),
            P("req", "mlp"),
            P("mlp", "req"),
        ),
        out_specs=P(("req", "mlp"), None),
        check_vma=False,
    )
```

```python
import jax
import jax.numpy as jnp
from jax import lax
from jax.sharding import PartitionSpec as P

HD = 104
MLP_CHUNKS = 4


def rms_scale(values, gain):
    wide = values.astype(jnp.float32)
    power = jnp.mean(wide * wide, axis=-1, keepdims=True)
    return wide * lax.rsqrt(power + 1e-06) * gain


def reduce_pieces(part, axis, count):
    pieces = lax.all_to_all(part.reshape((count, -1) + part.shape[1:]), axis, 0, 0, tiled=True)
    return jnp.sum(pieces.astype(jnp.float32), axis=0)


def gather_pieces(share, axis, count):
    spread = jnp.broadcast_to(share[None], (count,) + share.shape)
    return lax.all_to_all(spread, axis, 0, 0, tiled=True).reshape((-1,) + share.shape[1:])


def shards(
    patches, vis_gain, vis_proj, targets, lengths, text, attn_gain, wqkv, wo, mlp_gain, w_in, w_out
):
    requests = lax.axis_size("req")
    n_mlp = lax.axis_size("mlp")
    group = lax.axis_index("mlp")
    me = lax.axis_index("req")
    seq_len = text.shape[0]
    width = text.shape[1]
    merged_count = patches.shape[0]
    capacity = 2 * merged_count // requests

    in_rows = w_in.shape[0]
    blocks = lax.all_gather(jnp.stack([w_in, w_out.T], axis=0), "req", axis=0)
    all_targets = lax.all_gather(targets, "req", axis=0)

    patch_norm = rms_scale(patches[:, 0, :], vis_gain).astype(jnp.bfloat16)
    partial_value = jnp.dot(patch_norm, vis_proj, preferred_element_type=jnp.float32)
    vis_mine = reduce_pieces(partial_value, "mlp", n_mlp).astype(jnp.bfloat16)
    image_rows = gather_pieces(vis_mine, "mlp", n_mlp)

    target_req = targets // seq_len
    one_hot = (target_req[:, None] == jnp.arange(requests)[None, :]).astype(jnp.int32)
    before = jnp.cumsum(one_hot, axis=0) - one_hot
    rank_in = jnp.sum(before * one_hot, axis=1)
    slot_ids = target_req * capacity + rank_in
    buffer = jnp.zeros((requests * capacity, width), jnp.bfloat16).at[slot_ids].set(image_rows)
    buffer = buffer.reshape(requests, capacity, width)
    received = lax.all_to_all(buffer, "req", split_axis=0, concat_axis=0, tiled=True)
    arrived = received.reshape(requests * capacity, width)

    mine = (all_targets // seq_len) == me
    mine_i = mine.astype(jnp.int32)
    rank_here = jnp.cumsum(mine_i, axis=1) - mine_i
    src_ids = jnp.arange(requests, dtype=jnp.int32)[:, None]
    where_to = jnp.where(mine, src_ids * capacity + rank_here, requests * capacity)
    flat_slots = (
        jnp.full((requests * capacity,), seq_len, jnp.int32)
        .at[where_to.reshape(-1)]
        .set((all_targets % seq_len).reshape(-1), mode="drop")
    )
    embedded = text.at[flat_slots].set(arrived, mode="drop")

    attn_in = rms_scale(embedded, attn_gain).astype(jnp.bfloat16)
    qkv = jnp.dot(attn_in, wqkv, preferred_element_type=jnp.float32).astype(jnp.bfloat16)
    local_heads = wqkv.shape[1] // (3 * HD)
    qkv = qkv.reshape(seq_len, local_heads, 3, HD)
    query, keys, values = (qkv[:, :, 0], qkv[:, :, 1], qkv[:, :, 2])
    scores = (
        jnp.einsum("qhd,khd->hqk", query, keys, preferred_element_type=jnp.float32)
        / jnp.float32(HD) ** 0.5
    )
    row_ids = jnp.arange(seq_len)
    causal = row_ids[None, :] <= row_ids[:, None]
    scores = jnp.where(causal[None], scores, jnp.float32(-1e30))
    peak = jnp.max(scores, axis=-1, keepdims=True)
    weights = jnp.exp(scores - peak)
    probs = (weights / jnp.sum(weights, axis=-1, keepdims=True)).astype(jnp.bfloat16)
    context = jnp.einsum("hqk,khd->qhd", probs, values, preferred_element_type=jnp.float32).astype(
        jnp.bfloat16
    )
    context = context.reshape(seq_len, local_heads * HD)
    attn_part = jnp.dot(context, wo, preferred_element_type=jnp.float32).astype(jnp.bfloat16)
    share_rows = seq_len // n_mlp
    share_start = group * share_rows
    attn_pieces = lax.all_to_all(
        attn_part.reshape(n_mlp, share_rows, width), "mlp", 0, 0, tiled=True
    )
    w_in_full = blocks[:, 0].reshape(-1, w_in.shape[1])
    w_out_t = blocks[:, 1].reshape(-1, w_in.shape[1])
    attn_pieces, w_in_full, w_out_t = lax.optimization_barrier((attn_pieces, w_in_full, w_out_t))
    embedded_share = lax.dynamic_slice_in_dim(embedded, share_start, share_rows, 0)
    resid_share = embedded_share.astype(jnp.float32) + jnp.sum(
        attn_pieces.astype(jnp.float32), axis=0
    )
    mlp_in_share = rms_scale(resid_share, mlp_gain).astype(jnp.bfloat16)

    sub = share_rows // MLP_CHUNKS
    outs = []
    for chunk in range(MLP_CHUNKS):
        rows_in = gather_pieces(mlp_in_share[chunk * sub : (chunk + 1) * sub], "mlp", n_mlp)
        upward = jnp.dot(rows_in, w_in_full, preferred_element_type=jnp.float32)
        active = jax.nn.gelu(upward, approximate=False).astype(jnp.bfloat16)
        mlp_part = lax.dot_general(
            active, w_out_t, (((1,), (1,)), ((), ())), preferred_element_type=jnp.float32
        ).astype(jnp.bfloat16)
        outs.append(reduce_pieces(mlp_part, "mlp", n_mlp))
    result = resid_share + jnp.concatenate(outs, axis=0)
    share_ids = share_start + jnp.arange(share_rows)
    valid = share_ids < lengths[0]
    return jnp.where(valid[:, None], result, jnp.float32(0.0)).astype(jnp.bfloat16)


def solution(mesh):
    return jax.shard_map(
        shards,
        mesh=mesh,
        in_specs=(
            P("req", "mlp", None),
            P(),
            P("mlp", None),
            P("req"),
            P("req"),
            P("req", None),
            P(),
            P(None, "mlp"),
            P("mlp", None),
            P(),
            P("req", "mlp"),
            P("mlp", "req"),
        ),
        out_specs=P(("req", "mlp"), None),
        check_vma=False,
    )
```

```python
import jax
import jax.numpy as jnp
from jax import lax
from jax.sharding import PartitionSpec as P

HD = 104
MLP_CHUNKS = 2
TAG = 128


def rms_scale(values, gain):
    wide = values.astype(jnp.float32)
    power = jnp.mean(wide * wide, axis=-1, keepdims=True)
    return wide * lax.rsqrt(power + 1e-06) * gain


def reduce_pieces(part, axis, count):
    pieces = lax.all_to_all(part.reshape((count, -1) + part.shape[1:]), axis, 0, 0, tiled=True)
    return jnp.sum(pieces.astype(jnp.float32), axis=0)


def gather_pieces(share, axis, count):
    spread = jnp.broadcast_to(share[None], (count,) + share.shape)
    return lax.all_to_all(spread, axis, 0, 0, tiled=True).reshape((-1,) + share.shape[1:])


def shards(
    patches, vis_gain, vis_proj, targets, lengths, text, attn_gain, wqkv, wo, mlp_gain, w_in, w_out
):
    requests = lax.axis_size("req")
    n_mlp = lax.axis_size("mlp")
    group = lax.axis_index("mlp")
    me = lax.axis_index("req")
    seq_len = text.shape[0]
    width = text.shape[1]
    merged_count = patches.shape[0]
    capacity = 2 * merged_count // requests

    in_rows = w_in.shape[0]
    blocks = lax.all_gather(jnp.stack([w_in, w_out.T], axis=0), "req", axis=0)

    patch_norm = rms_scale(patches[:, 0, :], vis_gain).astype(jnp.bfloat16)
    partial_value = jnp.dot(patch_norm, vis_proj, preferred_element_type=jnp.float32)
    vis_mine = reduce_pieces(partial_value, "mlp", n_mlp).astype(jnp.bfloat16)
    image_rows = gather_pieces(vis_mine, "mlp", n_mlp)

    target_req = targets // seq_len
    position = targets % seq_len
    tag = jnp.stack(
        [position // 32, position % 32, jnp.ones_like(position)], axis=1
    ).astype(jnp.bfloat16)
    tagged = jnp.concatenate([image_rows, jnp.pad(tag, ((0, 0), (0, TAG - 3)))], axis=1)
    one_hot = (target_req[:, None] == jnp.arange(requests)[None, :]).astype(jnp.int32)
    before = jnp.cumsum(one_hot, axis=0) - one_hot
    rank_in = jnp.sum(before * one_hot, axis=1)
    slot_ids = target_req * capacity + rank_in
    buffer = jnp.zeros((requests * capacity, width + TAG), jnp.bfloat16).at[slot_ids].set(tagged)
    buffer = buffer.reshape(requests, capacity, width + TAG)
    received = lax.all_to_all(buffer, "req", split_axis=0, concat_axis=0, tiled=True)
    arrived = received.reshape(requests * capacity, width + TAG)
    got = arrived[:, width : width + 3].astype(jnp.int32)
    flat_slots = jnp.where(got[:, 2] > 0, got[:, 0] * 32 + got[:, 1], seq_len)
    embedded = text.at[flat_slots].set(arrived[:, :width], mode="drop")

    attn_in = rms_scale(embedded, attn_gain).astype(jnp.bfloat16)
    qkv = jnp.dot(attn_in, wqkv, preferred_element_type=jnp.float32).astype(jnp.bfloat16)
    local_heads = wqkv.shape[1] // (3 * HD)
    qkv = qkv.reshape(seq_len, local_heads, 3, HD)
    query, keys, values = (qkv[:, :, 0], qkv[:, :, 1], qkv[:, :, 2])
    scores = (
        jnp.einsum("qhd,khd->hqk", query, keys, preferred_element_type=jnp.float32)
        / jnp.float32(HD) ** 0.5
    )
    row_ids = jnp.arange(seq_len)
    causal = row_ids[None, :] <= row_ids[:, None]
    scores = jnp.where(causal[None], scores, jnp.float32(-1e30))
    peak = jnp.max(scores, axis=-1, keepdims=True)
    weights = jnp.exp(scores - peak)
    probs = (weights / jnp.sum(weights, axis=-1, keepdims=True)).astype(jnp.bfloat16)
    context = jnp.einsum("hqk,khd->qhd", probs, values, preferred_element_type=jnp.float32).astype(
        jnp.bfloat16
    )
    context = context.reshape(seq_len, local_heads * HD)
    attn_part = jnp.dot(context, wo, preferred_element_type=jnp.float32).astype(jnp.bfloat16)
    share_rows = seq_len // n_mlp
    share_start = group * share_rows
    attn_pieces = lax.all_to_all(
        attn_part.reshape(n_mlp, share_rows, width), "mlp", 0, 0, tiled=True
    )
    w_in_full = blocks[:, 0].reshape(-1, w_in.shape[1])
    w_out_t = blocks[:, 1].reshape(-1, w_in.shape[1])
    attn_pieces, w_in_full, w_out_t = lax.optimization_barrier((attn_pieces, w_in_full, w_out_t))
    embedded_share = lax.dynamic_slice_in_dim(embedded, share_start, share_rows, 0)
    resid_share = embedded_share.astype(jnp.float32) + jnp.sum(
        attn_pieces.astype(jnp.float32), axis=0
    )
    mlp_in_share = rms_scale(resid_share, mlp_gain).astype(jnp.bfloat16)

    mlp_in = gather_pieces(mlp_in_share, "mlp", n_mlp).reshape(n_mlp, share_rows, width)
    sub = share_rows // MLP_CHUNKS
    outs = []
    for chunk in range(MLP_CHUNKS):
        rows_in = mlp_in[:, chunk * sub : (chunk + 1) * sub].reshape(n_mlp * sub, width)
        upward = jnp.dot(rows_in, w_in_full, preferred_element_type=jnp.float32)
        active = jax.nn.gelu(upward, approximate=False).astype(jnp.bfloat16)
        mlp_part = lax.dot_general(
            active, w_out_t, (((1,), (1,)), ((), ())), preferred_element_type=jnp.float32
        ).astype(jnp.bfloat16)
        outs.append(reduce_pieces(mlp_part, "mlp", n_mlp))
    result = resid_share + jnp.concatenate(outs, axis=0)
    share_ids = share_start + jnp.arange(share_rows)
    valid = share_ids < lengths[0]
    return jnp.where(valid[:, None], result, jnp.float32(0.0)).astype(jnp.bfloat16)


def solution(mesh):
    return jax.shard_map(
        shards,
        mesh=mesh,
        in_specs=(
            P("req", "mlp", None),
            P(),
            P("mlp", None),
            P("req"),
            P("req"),
            P("req", None),
            P(),
            P(None, "mlp"),
            P("mlp", None),
            P(),
            P("req", "mlp"),
            P("mlp", "req"),
        ),
        out_specs=P(("req", "mlp"), None),
        check_vma=False,
    )
```

```python
import jax
import jax.numpy as jnp
from jax import lax
from jax.sharding import PartitionSpec as P

HD = 104
MLP_CHUNKS = 2
TAG = 128


def rms_scale(values, gain):
    wide = values.astype(jnp.float32)
    power = jnp.mean(wide * wide, axis=-1, keepdims=True)
    return wide * lax.rsqrt(power + 1e-06) * gain


def reduce_pieces(part, axis, count):
    pieces = lax.all_to_all(part.reshape((count, -1) + part.shape[1:]), axis, 0, 0, tiled=True)
    return jnp.sum(pieces.astype(jnp.float32), axis=0)


def gather_pieces(share, axis, count):
    spread = jnp.broadcast_to(share[None], (count,) + share.shape)
    return lax.all_to_all(spread, axis, 0, 0, tiled=True).reshape((-1,) + share.shape[1:])


def shards(
    patches, vis_gain, vis_proj, targets, lengths, text, attn_gain, wqkv, wo, mlp_gain, w_in, w_out
):
    requests = lax.axis_size("req")
    n_mlp = lax.axis_size("mlp")
    group = lax.axis_index("mlp")
    me = lax.axis_index("req")
    seq_len = text.shape[0]
    width = text.shape[1]
    merged_count = patches.shape[0]
    capacity = 2 * merged_count // requests

    in_rows = w_in.shape[0]
    blocks = lax.all_gather(jnp.stack([w_in, w_out.T], axis=0), "req", axis=0)

    patch_norm = rms_scale(patches[:, 0, :], vis_gain).astype(jnp.bfloat16)
    partial_value = jnp.dot(patch_norm, vis_proj, preferred_element_type=jnp.float32)
    vis_mine = reduce_pieces(partial_value, "mlp", n_mlp).astype(jnp.bfloat16)
    image_rows = gather_pieces(vis_mine, "mlp", n_mlp)

    target_req = targets // seq_len
    position = targets % seq_len
    tag = jnp.stack(
        [position // 32, position % 32, jnp.ones_like(position)], axis=1
    ).astype(jnp.bfloat16)
    tagged = jnp.concatenate([image_rows, jnp.pad(tag, ((0, 0), (0, TAG - 3)))], axis=1)
    one_hot = (target_req[:, None] == jnp.arange(requests)[None, :]).astype(jnp.int32)
    before = jnp.cumsum(one_hot, axis=0) - one_hot
    rank_in = jnp.sum(before * one_hot, axis=1)
    slot_ids = target_req * capacity + rank_in
    buffer = jnp.zeros((requests * capacity, width + TAG), jnp.bfloat16).at[slot_ids].set(tagged)
    buffer = buffer.reshape(requests, capacity, width + TAG)
    received = lax.all_to_all(buffer, "req", split_axis=0, concat_axis=0, tiled=True)
    arrived = received.reshape(requests * capacity, width + TAG)
    got = arrived[:, width : width + 3].astype(jnp.int32)
    flat_slots = jnp.where(got[:, 2] > 0, got[:, 0] * 32 + got[:, 1], seq_len)
    embedded = text.at[flat_slots].set(arrived[:, :width], mode="drop")

    attn_in = rms_scale(embedded, attn_gain).astype(jnp.bfloat16)
    qkv = jnp.dot(attn_in, wqkv, preferred_element_type=jnp.float32).astype(jnp.bfloat16)
    local_heads = wqkv.shape[1] // (3 * HD)
    qkv = qkv.reshape(seq_len, local_heads, 3, HD)
    query, keys, values = (qkv[:, :, 0], qkv[:, :, 1], qkv[:, :, 2])
    scores = (
        jnp.einsum("qhd,khd->hqk", query, keys, preferred_element_type=jnp.float32)
        / jnp.float32(HD) ** 0.5
    )
    share_rows = seq_len // n_mlp
    share_start = group * share_rows
    sub = share_rows // MLP_CHUNKS
    scale = jnp.float32(HD) ** 0.5
    row_ids = jnp.arange(seq_len).reshape(n_mlp, share_rows)
    key_ids = jnp.arange(seq_len)
    q_split = query.reshape(n_mlp, share_rows, local_heads, HD)
    w_in_full = blocks[:, 0].reshape(-1, w_in.shape[1])
    w_out_t = blocks[:, 1].reshape(-1, w_in.shape[1])
    embedded_share = lax.dynamic_slice_in_dim(embedded, share_start, share_rows, 0)
    outs = []
    for chunk in range(MLP_CHUNKS):
        q_rows = q_split[:, chunk * sub : (chunk + 1) * sub].reshape(n_mlp * sub, local_heads, HD)
        q_ids = row_ids[:, chunk * sub : (chunk + 1) * sub].reshape(-1)
        scores = (
            jnp.einsum("qhd,khd->hqk", q_rows, keys, preferred_element_type=jnp.float32) / scale
        )
        causal = key_ids[None, :] <= q_ids[:, None]
        scores = jnp.where(causal[None], scores, jnp.float32(-1e30))
        peak = jnp.max(scores, axis=-1, keepdims=True)
        weights = jnp.exp(scores - peak)
        probs = (weights / jnp.sum(weights, axis=-1, keepdims=True)).astype(jnp.bfloat16)
        context = jnp.einsum(
            "hqk,khd->qhd", probs, values, preferred_element_type=jnp.float32
        ).astype(jnp.bfloat16)
        context = context.reshape(n_mlp * sub, local_heads * HD)
        attn_part = jnp.dot(context, wo, preferred_element_type=jnp.float32).astype(jnp.bfloat16)
        attn_pieces = lax.all_to_all(
            attn_part.reshape(n_mlp, sub, width), "mlp", 0, 0, tiled=True
        )
        if chunk == 0:
            attn_pieces, w_in_full, w_out_t = lax.optimization_barrier(
                (attn_pieces, w_in_full, w_out_t)
            )
        resid_part = embedded_share[chunk * sub : (chunk + 1) * sub].astype(jnp.float32) + jnp.sum(
            attn_pieces.astype(jnp.float32), axis=0
        )
        mlp_in_part = rms_scale(resid_part, mlp_gain).astype(jnp.bfloat16)
        rows_in = gather_pieces(mlp_in_part, "mlp", n_mlp)
        upward = jnp.dot(rows_in, w_in_full, preferred_element_type=jnp.float32)
        active = jax.nn.gelu(upward, approximate=False).astype(jnp.bfloat16)
        mlp_part = lax.dot_general(
            active, w_out_t, (((1,), (1,)), ((), ())), preferred_element_type=jnp.float32
        ).astype(jnp.bfloat16)
        outs.append(resid_part + reduce_pieces(mlp_part, "mlp", n_mlp))
    result = jnp.concatenate(outs, axis=0)
    share_ids = share_start + jnp.arange(share_rows)
    valid = share_ids < lengths[0]
    return jnp.where(valid[:, None], result, jnp.float32(0.0)).astype(jnp.bfloat16)


def solution(mesh):
    return jax.shard_map(
        shards,
        mesh=mesh,
        in_specs=(
            P("req", "mlp", None),
            P(),
            P("mlp", None),
            P("req"),
            P("req"),
            P("req", None),
            P(),
            P(None, "mlp"),
            P("mlp", None),
            P(),
            P("req", "mlp"),
            P("mlp", "req"),
        ),
        out_specs=P(("req", "mlp"), None),
        check_vma=False,
    )
```

```python
import jax
import jax.numpy as jnp
from jax import lax
from jax.sharding import PartitionSpec as P

HD = 104
MLP_CHUNKS = 2
TAG = 128


def rms_scale(values, gain):
    wide = values.astype(jnp.float32)
    power = jnp.mean(wide * wide, axis=-1, keepdims=True)
    return wide * lax.rsqrt(power + 1e-06) * gain


def reduce_pieces(part, axis, count):
    pieces = lax.all_to_all(part.reshape((count, -1) + part.shape[1:]), axis, 0, 0, tiled=True)
    return jnp.sum(pieces.astype(jnp.float32), axis=0)


def gather_pieces(share, axis, count):
    spread = jnp.broadcast_to(share[None], (count,) + share.shape)
    return lax.all_to_all(spread, axis, 0, 0, tiled=True).reshape((-1,) + share.shape[1:])


def shards(
    patches, vis_gain, vis_proj, targets, lengths, text, attn_gain, wqkv, wo, mlp_gain, w_in, w_out
):
    requests = lax.axis_size("req")
    n_mlp = lax.axis_size("mlp")
    group = lax.axis_index("mlp")
    me = lax.axis_index("req")
    seq_len = text.shape[0]
    width = text.shape[1]
    merged_count = patches.shape[0]
    capacity = 2 * merged_count // requests

    in_rows = w_in.shape[0]
    hidden = w_in.shape[1]
    blocks = lax.all_gather(jnp.concatenate([w_in, w_out.T], axis=1), "req", axis=0)

    patch_norm = rms_scale(patches[:, 0, :], vis_gain).astype(jnp.bfloat16)
    partial_value = jnp.dot(patch_norm, vis_proj, preferred_element_type=jnp.float32)
    vis_mine = reduce_pieces(partial_value.astype(jnp.bfloat16), "mlp", n_mlp).astype(jnp.bfloat16)
    image_rows = gather_pieces(vis_mine, "mlp", n_mlp)

    target_req = targets // seq_len
    position = targets % seq_len
    tag = jnp.stack(
        [position // 32, position % 32, jnp.ones_like(position)], axis=1
    ).astype(jnp.bfloat16)
    tagged = jnp.concatenate([image_rows, jnp.pad(tag, ((0, 0), (0, TAG - 3)))], axis=1)
    one_hot = (target_req[:, None] == jnp.arange(requests)[None, :]).astype(jnp.int32)
    before = jnp.cumsum(one_hot, axis=0) - one_hot
    rank_in = jnp.sum(before * one_hot, axis=1)
    slot_ids = target_req * capacity + rank_in
    buffer = jnp.zeros((requests * capacity, width + TAG), jnp.bfloat16).at[slot_ids].set(tagged)
    buffer = buffer.reshape(requests, capacity, width + TAG)
    received = lax.all_to_all(buffer, "req", split_axis=0, concat_axis=0, tiled=True)
    weights_full = blocks.reshape(-1, 2 * hidden)
    received, weights_full = lax.optimization_barrier((received, weights_full))
    w_in_full = weights_full[:, :hidden]
    w_out_t = weights_full[:, hidden:]
    arrived = received.reshape(requests * capacity, width + TAG)
    got = arrived[:, width : width + 3].astype(jnp.int32)
    flat_slots = jnp.where(got[:, 2] > 0, got[:, 0] * 32 + got[:, 1], seq_len)
    embedded = text.at[flat_slots].set(arrived[:, :width], mode="drop")

    attn_in = rms_scale(embedded, attn_gain).astype(jnp.bfloat16)
    qkv = jnp.dot(attn_in, wqkv, preferred_element_type=jnp.float32).astype(jnp.bfloat16)
    local_heads = wqkv.shape[1] // (3 * HD)
    qkv = qkv.reshape(seq_len, local_heads, 3, HD)
    query, keys, values = (qkv[:, :, 0], qkv[:, :, 1], qkv[:, :, 2])
    scores = (
        jnp.einsum("qhd,khd->hqk", query, keys, preferred_element_type=jnp.float32)
        / jnp.float32(HD) ** 0.5
    )
    share_rows = seq_len // n_mlp
    share_start = group * share_rows
    sub = share_rows // MLP_CHUNKS
    scale = jnp.float32(HD) ** 0.5
    row_ids = jnp.arange(seq_len).reshape(n_mlp, share_rows)
    key_ids = jnp.arange(seq_len)
    q_split = query.reshape(n_mlp, share_rows, local_heads, HD)
    embedded_share = lax.dynamic_slice_in_dim(embedded, share_start, share_rows, 0)
    outs = []
    for chunk in range(MLP_CHUNKS):
        q_rows = q_split[:, chunk * sub : (chunk + 1) * sub].reshape(n_mlp * sub, local_heads, HD)
        q_ids = row_ids[:, chunk * sub : (chunk + 1) * sub].reshape(-1)
        scores = (
            jnp.einsum("qhd,khd->hqk", q_rows, keys, preferred_element_type=jnp.float32) / scale
        )
        causal = key_ids[None, :] <= q_ids[:, None]
        scores = jnp.where(causal[None], scores, jnp.float32(-1e30))
        peak = jnp.max(scores, axis=-1, keepdims=True)
        weights = jnp.exp(scores - peak)
        probs = (weights / jnp.sum(weights, axis=-1, keepdims=True)).astype(jnp.bfloat16)
        context = jnp.einsum(
            "hqk,khd->qhd", probs, values, preferred_element_type=jnp.float32
        ).astype(jnp.bfloat16)
        context = context.reshape(n_mlp * sub, local_heads * HD)
        attn_part = jnp.dot(context, wo, preferred_element_type=jnp.float32).astype(jnp.bfloat16)
        attn_pieces = lax.all_to_all(
            attn_part.reshape(n_mlp, sub, width), "mlp", 0, 0, tiled=True
        )
        resid_part = embedded_share[chunk * sub : (chunk + 1) * sub].astype(jnp.float32) + jnp.sum(
            attn_pieces.astype(jnp.float32), axis=0
        )
        mlp_in_part = rms_scale(resid_part, mlp_gain).astype(jnp.bfloat16)
        rows_in = gather_pieces(mlp_in_part, "mlp", n_mlp)
        upward = jnp.dot(rows_in, w_in_full, preferred_element_type=jnp.float32)
        active = jax.nn.gelu(upward, approximate=False).astype(jnp.bfloat16)
        mlp_part = lax.dot_general(
            active, w_out_t, (((1,), (1,)), ((), ())), preferred_element_type=jnp.float32
        ).astype(jnp.bfloat16)
        outs.append(resid_part + reduce_pieces(mlp_part, "mlp", n_mlp))
    result = jnp.concatenate(outs, axis=0)
    share_ids = share_start + jnp.arange(share_rows)
    valid = share_ids < lengths[0]
    return jnp.where(valid[:, None], result, jnp.float32(0.0)).astype(jnp.bfloat16)


def solution(mesh):
    return jax.shard_map(
        shards,
        mesh=mesh,
        in_specs=(
            P("req", "mlp", None),
            P(),
            P("mlp", None),
            P("req"),
            P("req"),
            P("req", None),
            P(),
            P(None, "mlp"),
            P("mlp", None),
            P(),
            P("req", "mlp"),
            P("mlp", "req"),
        ),
        out_specs=P(("req", "mlp"), None),
        check_vma=False,
    )
```

```python
import jax
import jax.numpy as jnp
from jax import lax
from jax.sharding import PartitionSpec as P

HD = 104
MLP_CHUNKS = 2
TAG = 128


def rms_scale(values, gain):
    wide = values.astype(jnp.float32)
    power = jnp.mean(wide * wide, axis=-1, keepdims=True)
    return wide * lax.rsqrt(power + 1e-06) * gain


def reduce_pieces(part, axis, count):
    pieces = lax.all_to_all(part.reshape((count, -1) + part.shape[1:]), axis, 0, 0, tiled=True)
    return jnp.sum(pieces.astype(jnp.float32), axis=0)


def gather_pieces(share, axis, count):
    spread = jnp.broadcast_to(share[None], (count,) + share.shape)
    return lax.all_to_all(spread, axis, 0, 0, tiled=True).reshape((-1,) + share.shape[1:])


def shards(
    patches, vis_gain, vis_proj, targets, lengths, text, attn_gain, wqkv, wo, mlp_gain, w_in, w_out
):
    requests = lax.axis_size("req")
    n_mlp = lax.axis_size("mlp")
    group = lax.axis_index("mlp")
    me = lax.axis_index("req")
    seq_len = text.shape[0]
    width = text.shape[1]
    merged_count = patches.shape[0]
    capacity = 2 * merged_count // requests

    in_rows = w_in.shape[0]
    hidden = w_in.shape[1]
    blocks = lax.all_gather(jnp.concatenate([w_in, w_out.T], axis=1), "req", axis=0)

    patch_norm = rms_scale(patches[:, 0, :], vis_gain).astype(jnp.bfloat16)
    partial_value = jnp.dot(patch_norm, vis_proj, preferred_element_type=jnp.float32)
    vis_mine = reduce_pieces(partial_value.astype(jnp.bfloat16), "mlp", n_mlp).astype(jnp.bfloat16)
    image_rows = gather_pieces(vis_mine, "mlp", n_mlp)

    target_req = targets // seq_len
    position = targets % seq_len
    tag = jnp.stack(
        [position // 32, position % 32, jnp.ones_like(position)], axis=1
    ).astype(jnp.bfloat16)
    tagged = jnp.concatenate([image_rows, jnp.pad(tag, ((0, 0), (0, TAG - 3)))], axis=1)
    one_hot = (target_req[:, None] == jnp.arange(requests)[None, :]).astype(jnp.int32)
    before = jnp.cumsum(one_hot, axis=0) - one_hot
    rank_in = jnp.sum(before * one_hot, axis=1)
    slot_ids = target_req * capacity + rank_in
    buffer = jnp.zeros((requests * capacity, width + TAG), jnp.bfloat16).at[slot_ids].set(tagged)
    buffer = buffer.reshape(requests, capacity, width + TAG)
    received = lax.all_to_all(buffer, "req", split_axis=0, concat_axis=0, tiled=True)
    arrived = received.reshape(requests * capacity, width + TAG)
    got = arrived[:, width : width + 3].astype(jnp.int32)
    flat_slots = jnp.where(got[:, 2] > 0, got[:, 0] * 32 + got[:, 1], seq_len)
    embedded = text.at[flat_slots].set(arrived[:, :width], mode="drop")

    attn_in = rms_scale(embedded, attn_gain).astype(jnp.bfloat16)
    qkv = jnp.dot(attn_in, wqkv, preferred_element_type=jnp.float32).astype(jnp.bfloat16)
    local_heads = wqkv.shape[1] // (3 * HD)
    qkv = qkv.reshape(seq_len, local_heads, 3, HD)
    query, keys, values = (qkv[:, :, 0], qkv[:, :, 1], qkv[:, :, 2])
    scores = (
        jnp.einsum("qhd,khd->hqk", query, keys, preferred_element_type=jnp.float32)
        / jnp.float32(HD) ** 0.5
    )
    share_rows = seq_len // n_mlp
    share_start = group * share_rows
    sub = share_rows // MLP_CHUNKS
    scale = jnp.float32(HD) ** 0.5
    row_ids = jnp.arange(seq_len).reshape(n_mlp, share_rows)
    key_ids = jnp.arange(seq_len)
    q_split = query.reshape(n_mlp, share_rows, local_heads, HD)
    embedded_share = lax.dynamic_slice_in_dim(embedded, share_start, share_rows, 0)
    resids, gathered = [], []
    for chunk in range(MLP_CHUNKS):
        q_rows = q_split[:, chunk * sub : (chunk + 1) * sub].reshape(n_mlp * sub, local_heads, HD)
        q_ids = row_ids[:, chunk * sub : (chunk + 1) * sub].reshape(-1)
        scores = (
            jnp.einsum("qhd,khd->hqk", q_rows, keys, preferred_element_type=jnp.float32) / scale
        )
        causal = key_ids[None, :] <= q_ids[:, None]
        scores = jnp.where(causal[None], scores, jnp.float32(-1e30))
        peak = jnp.max(scores, axis=-1, keepdims=True)
        weights = jnp.exp(scores - peak)
        probs = (weights / jnp.sum(weights, axis=-1, keepdims=True)).astype(jnp.bfloat16)
        context = jnp.einsum(
            "hqk,khd->qhd", probs, values, preferred_element_type=jnp.float32
        ).astype(jnp.bfloat16)
        context = context.reshape(n_mlp * sub, local_heads * HD)
        attn_part = jnp.dot(context, wo, preferred_element_type=jnp.float32).astype(jnp.bfloat16)
        attn_pieces = lax.all_to_all(
            attn_part.reshape(n_mlp, sub, width), "mlp", 0, 0, tiled=True
        )
        if chunk == MLP_CHUNKS - 1:
            weights_full = blocks.reshape(-1, 2 * hidden)
            attn_pieces, weights_full = lax.optimization_barrier((attn_pieces, weights_full))
        resid_part = embedded_share[chunk * sub : (chunk + 1) * sub].astype(jnp.float32) + jnp.sum(
            attn_pieces.astype(jnp.float32), axis=0
        )
        mlp_in_part = rms_scale(resid_part, mlp_gain).astype(jnp.bfloat16)
        resids.append(resid_part)
        gathered.append(gather_pieces(mlp_in_part, "mlp", n_mlp))
    w_in_full = weights_full[:, :hidden]
    w_out_t = weights_full[:, hidden:]
    outs = []
    for resid_part, rows_in in zip(resids, gathered):
        upward = jnp.dot(rows_in, w_in_full, preferred_element_type=jnp.float32)
        active = jax.nn.gelu(upward, approximate=False).astype(jnp.bfloat16)
        mlp_part = lax.dot_general(
            active, w_out_t, (((1,), (1,)), ((), ())), preferred_element_type=jnp.float32
        ).astype(jnp.bfloat16)
        outs.append(resid_part + reduce_pieces(mlp_part, "mlp", n_mlp))
    result = jnp.concatenate(outs, axis=0)
    share_ids = share_start + jnp.arange(share_rows)
    valid = share_ids < lengths[0]
    return jnp.where(valid[:, None], result, jnp.float32(0.0)).astype(jnp.bfloat16)


def solution(mesh):
    return jax.shard_map(
        shards,
        mesh=mesh,
        in_specs=(
            P("req", "mlp", None),
            P(),
            P("mlp", None),
            P("req"),
            P("req"),
            P("req", None),
            P(),
            P(None, "mlp"),
            P("mlp", None),
            P(),
            P("req", "mlp"),
            P("mlp", "req"),
        ),
        out_specs=P(("req", "mlp"), None),
        check_vma=False,
    )
```

```python
import jax
import jax.numpy as jnp
from jax import lax
from jax.sharding import PartitionSpec as P

HD = 104
MLP_CHUNKS = 2
TAG = 128


def rms_scale(values, gain):
    wide = values.astype(jnp.float32)
    power = jnp.mean(wide * wide, axis=-1, keepdims=True)
    return wide * lax.rsqrt(power + 1e-06) * gain


def reduce_pieces(part, axis, count):
    pieces = lax.all_to_all(part.reshape((count, -1) + part.shape[1:]), axis, 0, 0, tiled=True)
    return jnp.sum(pieces.astype(jnp.float32), axis=0)


def gather_pieces(share, axis, count):
    spread = jnp.broadcast_to(share[None], (count,) + share.shape)
    return lax.all_to_all(spread, axis, 0, 0, tiled=True).reshape((-1,) + share.shape[1:])


def shards(
    patches, vis_gain, vis_proj, targets, lengths, text, attn_gain, wqkv, wo, mlp_gain, w_in, w_out
):
    requests = lax.axis_size("req")
    n_mlp = lax.axis_size("mlp")
    group = lax.axis_index("mlp")
    me = lax.axis_index("req")
    seq_len = text.shape[0]
    width = text.shape[1]
    merged_count = patches.shape[0]
    capacity = 2 * merged_count // requests

    in_rows = w_in.shape[0]
    hidden = w_in.shape[1]
    in_blocks = lax.all_gather(w_in, "req", axis=0)

    patch_norm = rms_scale(patches[:, 0, :], vis_gain).astype(jnp.bfloat16)
    partial_value = jnp.dot(patch_norm, vis_proj, preferred_element_type=jnp.float32)
    vis_mine = reduce_pieces(partial_value.astype(jnp.bfloat16), "mlp", n_mlp).astype(jnp.bfloat16)
    image_rows = gather_pieces(vis_mine, "mlp", n_mlp)

    target_req = targets // seq_len
    position = targets % seq_len
    tag = jnp.stack(
        [position // 32, position % 32, jnp.ones_like(position)], axis=1
    ).astype(jnp.bfloat16)
    tagged = jnp.concatenate([image_rows, jnp.pad(tag, ((0, 0), (0, TAG - 3)))], axis=1)
    one_hot = (target_req[:, None] == jnp.arange(requests)[None, :]).astype(jnp.int32)
    before = jnp.cumsum(one_hot, axis=0) - one_hot
    rank_in = jnp.sum(before * one_hot, axis=1)
    slot_ids = target_req * capacity + rank_in
    buffer = jnp.zeros((requests * capacity, width + TAG), jnp.bfloat16).at[slot_ids].set(tagged)
    buffer = buffer.reshape(requests, capacity, width + TAG)
    received = lax.all_to_all(buffer, "req", split_axis=0, concat_axis=0, tiled=True)
    received, w_in_full, out_local = lax.optimization_barrier(
        (received, in_blocks.reshape(-1, hidden), w_out.T)
    )
    out_blocks = lax.all_gather(out_local, "req", axis=0)
    arrived = received.reshape(requests * capacity, width + TAG)
    got = arrived[:, width : width + 3].astype(jnp.int32)
    flat_slots = jnp.where(got[:, 2] > 0, got[:, 0] * 32 + got[:, 1], seq_len)
    embedded = text.at[flat_slots].set(arrived[:, :width], mode="drop")

    attn_in = rms_scale(embedded, attn_gain).astype(jnp.bfloat16)
    qkv = jnp.dot(attn_in, wqkv, preferred_element_type=jnp.float32).astype(jnp.bfloat16)
    local_heads = wqkv.shape[1] // (3 * HD)
    qkv = qkv.reshape(seq_len, local_heads, 3, HD)
    query, keys, values = (qkv[:, :, 0], qkv[:, :, 1], qkv[:, :, 2])
    scores = (
        jnp.einsum("qhd,khd->hqk", query, keys, preferred_element_type=jnp.float32)
        / jnp.float32(HD) ** 0.5
    )
    share_rows = seq_len // n_mlp
    share_start = group * share_rows
    sub = share_rows // MLP_CHUNKS
    scale = jnp.float32(HD) ** 0.5
    row_ids = jnp.arange(seq_len).reshape(n_mlp, share_rows)
    key_ids = jnp.arange(seq_len)
    q_split = query.reshape(n_mlp, share_rows, local_heads, HD)
    embedded_share = lax.dynamic_slice_in_dim(embedded, share_start, share_rows, 0)
    resids, gathered = [], []
    for chunk in range(MLP_CHUNKS):
        q_rows = q_split[:, chunk * sub : (chunk + 1) * sub].reshape(n_mlp * sub, local_heads, HD)
        q_ids = row_ids[:, chunk * sub : (chunk + 1) * sub].reshape(-1)
        scores = (
            jnp.einsum("qhd,khd->hqk", q_rows, keys, preferred_element_type=jnp.float32) / scale
        )
        causal = key_ids[None, :] <= q_ids[:, None]
        scores = jnp.where(causal[None], scores, jnp.float32(-1e30))
        peak = jnp.max(scores, axis=-1, keepdims=True)
        weights = jnp.exp(scores - peak)
        probs = (weights / jnp.sum(weights, axis=-1, keepdims=True)).astype(jnp.bfloat16)
        context = jnp.einsum(
            "hqk,khd->qhd", probs, values, preferred_element_type=jnp.float32
        ).astype(jnp.bfloat16)
        context = context.reshape(n_mlp * sub, local_heads * HD)
        attn_part = jnp.dot(context, wo, preferred_element_type=jnp.float32).astype(jnp.bfloat16)
        attn_pieces = lax.all_to_all(
            attn_part.reshape(n_mlp, sub, width), "mlp", 0, 0, tiled=True
        )
        if chunk == MLP_CHUNKS - 1:
            attn_pieces, w_out_t = lax.optimization_barrier(
                (attn_pieces, out_blocks.reshape(-1, hidden))
            )
        resid_part = embedded_share[chunk * sub : (chunk + 1) * sub].astype(jnp.float32) + jnp.sum(
            attn_pieces.astype(jnp.float32), axis=0
        )
        mlp_in_part = rms_scale(resid_part, mlp_gain).astype(jnp.bfloat16)
        resids.append(resid_part)
        gathered.append(gather_pieces(mlp_in_part, "mlp", n_mlp))
    outs = []
    for resid_part, rows_in in zip(resids, gathered):
        upward = jnp.dot(rows_in, w_in_full, preferred_element_type=jnp.float32)
        active = jax.nn.gelu(upward, approximate=False).astype(jnp.bfloat16)
        mlp_part = lax.dot_general(
            active, w_out_t, (((1,), (1,)), ((), ())), preferred_element_type=jnp.float32
        ).astype(jnp.bfloat16)
        outs.append(resid_part + reduce_pieces(mlp_part, "mlp", n_mlp))
    result = jnp.concatenate(outs, axis=0)
    share_ids = share_start + jnp.arange(share_rows)
    valid = share_ids < lengths[0]
    return jnp.where(valid[:, None], result, jnp.float32(0.0)).astype(jnp.bfloat16)


def solution(mesh):
    return jax.shard_map(
        shards,
        mesh=mesh,
        in_specs=(
            P("req", "mlp", None),
            P(),
            P("mlp", None),
            P("req"),
            P("req"),
            P("req", None),
            P(),
            P(None, "mlp"),
            P("mlp", None),
            P(),
            P("req", "mlp"),
            P("mlp", "req"),
        ),
        out_specs=P(("req", "mlp"), None),
        check_vma=False,
    )
```

```python
import jax
import jax.numpy as jnp
from jax import lax
from jax.sharding import PartitionSpec as P

HD = 104
MLP_CHUNKS = 2
TAG = 128


def rms_scale(values, gain):
    wide = values.astype(jnp.float32)
    power = jnp.mean(wide * wide, axis=-1, keepdims=True)
    return wide * lax.rsqrt(power + 1e-06) * gain


def reduce_pieces(part, axis, count):
    pieces = lax.all_to_all(part.reshape((count, -1) + part.shape[1:]), axis, 0, 0, tiled=True)
    return jnp.sum(pieces.astype(jnp.float32), axis=0)


def gather_pieces(share, axis, count):
    spread = jnp.broadcast_to(share[None], (count,) + share.shape)
    return lax.all_to_all(spread, axis, 0, 0, tiled=True).reshape((-1,) + share.shape[1:])


def shards(
    patches, vis_gain, vis_proj, targets, lengths, text, attn_gain, wqkv, wo, mlp_gain, w_in, w_out
):
    requests = lax.axis_size("req")
    n_mlp = lax.axis_size("mlp")
    group = lax.axis_index("mlp")
    me = lax.axis_index("req")
    seq_len = text.shape[0]
    width = text.shape[1]
    merged_count = patches.shape[0]
    capacity = 2 * merged_count // requests

    in_rows = w_in.shape[0]
    hidden = w_in.shape[1]
    in_blocks = lax.all_gather(w_in, "req", axis=0)
    wo_full = lax.all_gather(wo, "mlp", axis=0)

    patch_norm = rms_scale(patches[:, 0, :], vis_gain).astype(jnp.bfloat16)
    partial_value = jnp.dot(patch_norm, vis_proj, preferred_element_type=jnp.float32)
    vis_mine = reduce_pieces(partial_value.astype(jnp.bfloat16), "mlp", n_mlp).astype(jnp.bfloat16)
    image_rows = gather_pieces(vis_mine, "mlp", n_mlp)

    target_req = targets // seq_len
    position = targets % seq_len
    tag = jnp.stack(
        [position // 32, position % 32, jnp.ones_like(position)], axis=1
    ).astype(jnp.bfloat16)
    tagged = jnp.concatenate([image_rows, jnp.pad(tag, ((0, 0), (0, TAG - 3)))], axis=1)
    one_hot = (target_req[:, None] == jnp.arange(requests)[None, :]).astype(jnp.int32)
    before = jnp.cumsum(one_hot, axis=0) - one_hot
    rank_in = jnp.sum(before * one_hot, axis=1)
    slot_ids = target_req * capacity + rank_in
    buffer = jnp.zeros((requests * capacity, width + TAG), jnp.bfloat16).at[slot_ids].set(tagged)
    buffer = buffer.reshape(requests, capacity, width + TAG)
    received = lax.all_to_all(buffer, "req", split_axis=0, concat_axis=0, tiled=True)
    received, w_in_full, out_local = lax.optimization_barrier(
        (received, in_blocks.reshape(-1, hidden), w_out.T)
    )
    out_blocks = lax.all_gather(out_local, "req", axis=0)
    arrived = received.reshape(requests * capacity, width + TAG)
    got = arrived[:, width : width + 3].astype(jnp.int32)
    flat_slots = jnp.where(got[:, 2] > 0, got[:, 0] * 32 + got[:, 1], seq_len)
    embedded = text.at[flat_slots].set(arrived[:, :width], mode="drop")

    attn_in = rms_scale(embedded, attn_gain).astype(jnp.bfloat16)
    qkv = jnp.dot(attn_in, wqkv, preferred_element_type=jnp.float32).astype(jnp.bfloat16)
    local_heads = wqkv.shape[1] // (3 * HD)
    qkv = qkv.reshape(seq_len, local_heads, 3, HD)
    query, keys, values = (qkv[:, :, 0], qkv[:, :, 1], qkv[:, :, 2])
    scores = (
        jnp.einsum("qhd,khd->hqk", query, keys, preferred_element_type=jnp.float32)
        / jnp.float32(HD) ** 0.5
    )
    share_rows = seq_len // n_mlp
    share_start = group * share_rows
    sub = share_rows // MLP_CHUNKS
    scale = jnp.float32(HD) ** 0.5
    row_ids = jnp.arange(seq_len).reshape(n_mlp, share_rows)
    key_ids = jnp.arange(seq_len)
    q_split = query.reshape(n_mlp, share_rows, local_heads, HD)
    embedded_share = lax.dynamic_slice_in_dim(embedded, share_start, share_rows, 0)
    resids, gathered = [], []
    for chunk in range(MLP_CHUNKS):
        q_rows = q_split[:, chunk * sub : (chunk + 1) * sub].reshape(n_mlp * sub, local_heads, HD)
        q_ids = row_ids[:, chunk * sub : (chunk + 1) * sub].reshape(-1)
        scores = (
            jnp.einsum("qhd,khd->hqk", q_rows, keys, preferred_element_type=jnp.float32) / scale
        )
        causal = key_ids[None, :] <= q_ids[:, None]
        scores = jnp.where(causal[None], scores, jnp.float32(-1e30))
        peak = jnp.max(scores, axis=-1, keepdims=True)
        weights = jnp.exp(scores - peak)
        probs = (weights / jnp.sum(weights, axis=-1, keepdims=True)).astype(jnp.bfloat16)
        context = jnp.einsum(
            "hqk,khd->qhd", probs, values, preferred_element_type=jnp.float32
        ).astype(jnp.bfloat16)
        context = context.reshape(n_mlp, sub, local_heads * HD)
        contexts = lax.all_to_all(context, "mlp", 0, 0, tiled=True)
        attn_pieces = jnp.einsum(
            "sqc,scd->sqd", contexts, wo_full, preferred_element_type=jnp.float32
        ).astype(jnp.bfloat16)
        if chunk == MLP_CHUNKS - 1:
            attn_pieces, w_out_t = lax.optimization_barrier(
                (attn_pieces, out_blocks.reshape(-1, hidden))
            )
        resid_part = embedded_share[chunk * sub : (chunk + 1) * sub].astype(jnp.float32) + jnp.sum(
            attn_pieces.astype(jnp.float32), axis=0
        )
        mlp_in_part = rms_scale(resid_part, mlp_gain).astype(jnp.bfloat16)
        resids.append(resid_part)
        gathered.append(gather_pieces(mlp_in_part, "mlp", n_mlp))
    outs = []
    for resid_part, rows_in in zip(resids, gathered):
        upward = jnp.dot(rows_in, w_in_full, preferred_element_type=jnp.float32)
        active = jax.nn.gelu(upward, approximate=False).astype(jnp.bfloat16)
        mlp_part = lax.dot_general(
            active, w_out_t, (((1,), (1,)), ((), ())), preferred_element_type=jnp.float32
        ).astype(jnp.bfloat16)
        outs.append(resid_part + reduce_pieces(mlp_part, "mlp", n_mlp))
    result = jnp.concatenate(outs, axis=0)
    share_ids = share_start + jnp.arange(share_rows)
    valid = share_ids < lengths[0]
    return jnp.where(valid[:, None], result, jnp.float32(0.0)).astype(jnp.bfloat16)


def solution(mesh):
    return jax.shard_map(
        shards,
        mesh=mesh,
        in_specs=(
            P("req", "mlp", None),
            P(),
            P("mlp", None),
            P("req"),
            P("req"),
            P("req", None),
            P(),
            P(None, "mlp"),
            P("mlp", None),
            P(),
            P("req", "mlp"),
            P("mlp", "req"),
        ),
        out_specs=P(("req", "mlp"), None),
        check_vma=False,
    )
```

```python
import jax
import jax.numpy as jnp
from jax import lax
from jax.sharding import PartitionSpec as P

HD = 104
MLP_CHUNKS = 2
TAG = 128


def rms_scale(values, gain):
    wide = values.astype(jnp.float32)
    power = jnp.mean(wide * wide, axis=-1, keepdims=True)
    return wide * lax.rsqrt(power + 1e-06) * gain


def reduce_pieces(part, axis, count):
    pieces = lax.all_to_all(part.reshape((count, -1) + part.shape[1:]), axis, 0, 0, tiled=True)
    return jnp.sum(pieces.astype(jnp.float32), axis=0)


def gather_pieces(share, axis, count):
    spread = jnp.broadcast_to(share[None], (count,) + share.shape)
    return lax.all_to_all(spread, axis, 0, 0, tiled=True).reshape((-1,) + share.shape[1:])


def shards(
    patches, vis_gain, vis_proj, targets, lengths, text, attn_gain, wqkv, wo, mlp_gain, w_in, w_out
):
    requests = lax.axis_size("req")
    n_mlp = lax.axis_size("mlp")
    group = lax.axis_index("mlp")
    me = lax.axis_index("req")
    seq_len = text.shape[0]
    width = text.shape[1]
    merged_count = patches.shape[0]
    capacity = 2 * merged_count // requests

    in_rows = w_in.shape[0]
    hidden = w_in.shape[1]
    in_blocks = lax.all_gather(w_in, "req", axis=0)

    patch_norm = rms_scale(patches[:, 0, :], vis_gain).astype(jnp.bfloat16)
    partial_value = jnp.dot(patch_norm, vis_proj, preferred_element_type=jnp.float32)
    vis_mine = reduce_pieces(partial_value.astype(jnp.bfloat16), "mlp", n_mlp).astype(jnp.bfloat16)
    image_rows = gather_pieces(vis_mine, "mlp", n_mlp)

    target_req = targets // seq_len
    position = targets % seq_len
    tag = jnp.stack(
        [position // 32, position % 32, jnp.ones_like(position)], axis=1
    ).astype(jnp.bfloat16)
    tagged = jnp.concatenate([image_rows, jnp.pad(tag, ((0, 0), (0, TAG - 3)))], axis=1)
    one_hot = (target_req[:, None] == jnp.arange(requests)[None, :]).astype(jnp.int32)
    before = jnp.cumsum(one_hot, axis=0) - one_hot
    rank_in = jnp.sum(before * one_hot, axis=1)
    slot_ids = target_req * capacity + rank_in
    buffer = jnp.zeros((requests * capacity, width + TAG), jnp.bfloat16).at[slot_ids].set(tagged)
    buffer = buffer.reshape(requests, capacity, width + TAG)
    received = lax.all_to_all(buffer, "req", split_axis=0, concat_axis=0, tiled=True)
    received, w_in_full, out_local = lax.optimization_barrier(
        (received, in_blocks.reshape(-1, hidden), w_out.T)
    )
    out_blocks = lax.all_gather(out_local, "req", axis=0)
    arrived = received.reshape(requests * capacity, width + TAG)
    got = arrived[:, width : width + 3].astype(jnp.int32)
    flat_slots = jnp.where(got[:, 2] > 0, got[:, 0] * 32 + got[:, 1], seq_len)
    arrivals = requests * capacity
    source_of = (
        jnp.full((seq_len,), arrivals, jnp.int32)
        .at[flat_slots]
        .set(jnp.arange(arrivals, dtype=jnp.int32), mode="drop")
    )
    picked = jnp.take(arrived[:, :width], jnp.minimum(source_of, arrivals - 1), axis=0)
    embedded = jnp.where((source_of < arrivals)[:, None], picked, text)

    attn_in = rms_scale(embedded, attn_gain).astype(jnp.bfloat16)
    qkv = jnp.dot(attn_in, wqkv, preferred_element_type=jnp.float32).astype(jnp.bfloat16)
    local_heads = wqkv.shape[1] // (3 * HD)
    qkv = qkv.reshape(seq_len, local_heads, 3, HD)
    query, keys, values = (qkv[:, :, 0], qkv[:, :, 1], qkv[:, :, 2])
    scores = (
        jnp.einsum("qhd,khd->hqk", query, keys, preferred_element_type=jnp.float32)
        / jnp.float32(HD) ** 0.5
    )
    share_rows = seq_len // n_mlp
    share_start = group * share_rows
    sub = share_rows // MLP_CHUNKS
    scale = jnp.float32(HD) ** 0.5
    row_ids = jnp.arange(seq_len).reshape(n_mlp, share_rows)
    key_ids = jnp.arange(seq_len)
    q_split = query.reshape(n_mlp, share_rows, local_heads, HD)
    embedded_share = lax.dynamic_slice_in_dim(embedded, share_start, share_rows, 0)
    resids, gathered = [], []
    for chunk in range(MLP_CHUNKS):
        q_rows = q_split[:, chunk * sub : (chunk + 1) * sub].reshape(n_mlp * sub, local_heads, HD)
        q_ids = row_ids[:, chunk * sub : (chunk + 1) * sub].reshape(-1)
        scores = (
            jnp.einsum("qhd,khd->hqk", q_rows, keys, preferred_element_type=jnp.float32) / scale
        )
        causal = key_ids[None, :] <= q_ids[:, None]
        scores = jnp.where(causal[None], scores, jnp.float32(-1e30))
        peak = jnp.max(scores, axis=-1, keepdims=True)
        weights = jnp.exp(scores - peak)
        probs = (weights / jnp.sum(weights, axis=-1, keepdims=True)).astype(jnp.bfloat16)
        context = jnp.einsum(
            "hqk,khd->qhd", probs, values, preferred_element_type=jnp.float32
        ).astype(jnp.bfloat16)
        context = context.reshape(n_mlp * sub, local_heads * HD)
        attn_part = jnp.dot(context, wo, preferred_element_type=jnp.float32).astype(jnp.bfloat16)
        attn_pieces = lax.all_to_all(
            attn_part.reshape(n_mlp, sub, width), "mlp", 0, 0, tiled=True
        )
        if chunk == MLP_CHUNKS - 1:
            attn_pieces, w_out_t = lax.optimization_barrier(
                (attn_pieces, out_blocks.reshape(-1, hidden))
            )
        resid_part = embedded_share[chunk * sub : (chunk + 1) * sub].astype(jnp.float32) + jnp.sum(
            attn_pieces.astype(jnp.float32), axis=0
        )
        mlp_in_part = rms_scale(resid_part, mlp_gain).astype(jnp.bfloat16)
        resids.append(resid_part)
        gathered.append(gather_pieces(mlp_in_part, "mlp", n_mlp))
    outs = []
    for resid_part, rows_in in zip(resids, gathered):
        upward = jnp.dot(rows_in, w_in_full, preferred_element_type=jnp.float32)
        active = jax.nn.gelu(upward, approximate=False).astype(jnp.bfloat16)
        mlp_part = lax.dot_general(
            active, w_out_t, (((1,), (1,)), ((), ())), preferred_element_type=jnp.float32
        ).astype(jnp.bfloat16)
        outs.append(resid_part + reduce_pieces(mlp_part, "mlp", n_mlp))
    result = jnp.concatenate(outs, axis=0)
    share_ids = share_start + jnp.arange(share_rows)
    valid = share_ids < lengths[0]
    return jnp.where(valid[:, None], result, jnp.float32(0.0)).astype(jnp.bfloat16)


def solution(mesh):
    return jax.shard_map(
        shards,
        mesh=mesh,
        in_specs=(
            P("req", "mlp", None),
            P(),
            P("mlp", None),
            P("req"),
            P("req"),
            P("req", None),
            P(),
            P(None, "mlp"),
            P("mlp", None),
            P(),
            P("req", "mlp"),
            P("mlp", "req"),
        ),
        out_specs=P(("req", "mlp"), None),
        check_vma=False,
    )
```

```python
import jax
import jax.numpy as jnp
from jax import lax
from jax.sharding import PartitionSpec as P

HD = 104
MLP_CHUNKS = 2
TAG = 128


def rms_scale(values, gain):
    wide = values.astype(jnp.float32)
    power = jnp.mean(wide * wide, axis=-1, keepdims=True)
    return wide * lax.rsqrt(power + 1e-06) * gain


def reduce_pieces(part, axis, count):
    pieces = lax.all_to_all(part.reshape((count, -1) + part.shape[1:]), axis, 0, 0, tiled=True)
    return jnp.sum(pieces.astype(jnp.float32), axis=0)


def gather_pieces(share, axis, count):
    spread = jnp.broadcast_to(share[None], (count,) + share.shape)
    return lax.all_to_all(spread, axis, 0, 0, tiled=True).reshape((-1,) + share.shape[1:])


def shards(
    patches, vis_gain, vis_proj, targets, lengths, text, attn_gain, wqkv, wo, mlp_gain, w_in, w_out
):
    requests = lax.axis_size("req")
    n_mlp = lax.axis_size("mlp")
    group = lax.axis_index("mlp")
    me = lax.axis_index("req")
    seq_len = text.shape[0]
    width = text.shape[1]
    merged_count = patches.shape[0]
    capacity = 2 * merged_count // requests

    in_rows = w_in.shape[0]
    hidden = w_in.shape[1]
    in_blocks = lax.all_gather(w_in, "req", axis=0)

    patch_norm = rms_scale(patches[:, 0, :], vis_gain).astype(jnp.bfloat16)
    partial_value = jnp.dot(patch_norm, vis_proj, preferred_element_type=jnp.float32)
    vis_mine = reduce_pieces(partial_value.astype(jnp.bfloat16), "mlp", n_mlp).astype(jnp.bfloat16)
    image_rows = gather_pieces(vis_mine, "mlp", n_mlp)

    target_req = targets // seq_len
    position = targets % seq_len
    tag = jnp.stack(
        [position // 32, position % 32, jnp.ones_like(position)], axis=1
    ).astype(jnp.bfloat16)
    tagged = jnp.concatenate([image_rows, jnp.pad(tag, ((0, 0), (0, TAG - 3)))], axis=1)
    one_hot = (target_req[:, None] == jnp.arange(requests)[None, :]).astype(jnp.int32)
    before = jnp.cumsum(one_hot, axis=0) - one_hot
    rank_in = jnp.sum(before * one_hot, axis=1)
    slot_ids = target_req * capacity + rank_in
    buffer = jnp.zeros((requests * capacity, width + TAG), jnp.bfloat16).at[slot_ids].set(tagged)
    buffer = buffer.reshape(requests, capacity, width + TAG)
    received = lax.all_to_all(buffer, "req", split_axis=0, concat_axis=0, tiled=True)
    text_qkv = jnp.dot(
        rms_scale(text, attn_gain).astype(jnp.bfloat16), wqkv, preferred_element_type=jnp.float32
    ).astype(jnp.bfloat16)
    received, w_in_full, out_local, text_qkv = lax.optimization_barrier(
        (received, in_blocks.reshape(-1, hidden), w_out.T, text_qkv)
    )
    out_blocks = lax.all_gather(out_local, "req", axis=0)
    arrived = received.reshape(requests * capacity, width + TAG)
    got = arrived[:, width : width + 3].astype(jnp.int32)
    flat_slots = jnp.where(got[:, 2] > 0, got[:, 0] * 32 + got[:, 1], seq_len)
    arrivals = requests * capacity
    source_of = (
        jnp.full((seq_len,), arrivals, jnp.int32)
        .at[flat_slots]
        .set(jnp.arange(arrivals, dtype=jnp.int32), mode="drop")
    )
    image_in = rms_scale(arrived[:, :width], attn_gain).astype(jnp.bfloat16)
    image_qkv = jnp.dot(image_in, wqkv, preferred_element_type=jnp.float32).astype(jnp.bfloat16)
    is_image = source_of < arrivals
    pick = jnp.minimum(source_of, arrivals - 1)
    qkv = jnp.where(is_image[:, None], jnp.take(image_qkv, pick, axis=0), text_qkv)
    local_heads = wqkv.shape[1] // (3 * HD)
    qkv = qkv.reshape(seq_len, local_heads, 3, HD)
    query, keys, values = (qkv[:, :, 0], qkv[:, :, 1], qkv[:, :, 2])
    share_rows = seq_len // n_mlp
    share_start = group * share_rows
    sub = share_rows // MLP_CHUNKS
    scale = jnp.float32(HD) ** 0.5
    row_ids = jnp.arange(seq_len).reshape(n_mlp, share_rows)
    key_ids = jnp.arange(seq_len)
    q_split = query.reshape(n_mlp, share_rows, local_heads, HD)
    share_pick = lax.dynamic_slice_in_dim(pick, share_start, share_rows, 0)
    share_image = lax.dynamic_slice_in_dim(is_image, share_start, share_rows, 0)
    embedded_share = jnp.where(
        share_image[:, None],
        jnp.take(arrived[:, :width], share_pick, axis=0),
        lax.dynamic_slice_in_dim(text, share_start, share_rows, 0),
    )
    resids, gathered = [], []
    for chunk in range(MLP_CHUNKS):
        q_rows = q_split[:, chunk * sub : (chunk + 1) * sub].reshape(n_mlp * sub, local_heads, HD)
        q_ids = row_ids[:, chunk * sub : (chunk + 1) * sub].reshape(-1)
        scores = (
            jnp.einsum("qhd,khd->hqk", q_rows, keys, preferred_element_type=jnp.float32) / scale
        )
        causal = key_ids[None, :] <= q_ids[:, None]
        scores = jnp.where(causal[None], scores, jnp.float32(-1e30))
        peak = jnp.max(scores, axis=-1, keepdims=True)
        weights = jnp.exp(scores - peak)
        probs = (weights / jnp.sum(weights, axis=-1, keepdims=True)).astype(jnp.bfloat16)
        context = jnp.einsum(
            "hqk,khd->qhd", probs, values, preferred_element_type=jnp.float32
        ).astype(jnp.bfloat16)
        context = context.reshape(n_mlp * sub, local_heads * HD)
        attn_part = jnp.dot(context, wo, preferred_element_type=jnp.float32).astype(jnp.bfloat16)
        attn_pieces = lax.all_to_all(
            attn_part.reshape(n_mlp, sub, width), "mlp", 0, 0, tiled=True
        )
        if chunk == MLP_CHUNKS - 1:
            attn_pieces, w_out_t = lax.optimization_barrier(
                (attn_pieces, out_blocks.reshape(-1, hidden))
            )
        resid_part = embedded_share[chunk * sub : (chunk + 1) * sub].astype(jnp.float32) + jnp.sum(
            attn_pieces.astype(jnp.float32), axis=0
        )
        mlp_in_part = rms_scale(resid_part, mlp_gain).astype(jnp.bfloat16)
        resids.append(resid_part)
        gathered.append(gather_pieces(mlp_in_part, "mlp", n_mlp))
    outs = []
    for resid_part, rows_in in zip(resids, gathered):
        upward = jnp.dot(rows_in, w_in_full, preferred_element_type=jnp.float32)
        active = jax.nn.gelu(upward, approximate=False).astype(jnp.bfloat16)
        mlp_part = lax.dot_general(
            active, w_out_t, (((1,), (1,)), ((), ())), preferred_element_type=jnp.float32
        ).astype(jnp.bfloat16)
        outs.append(resid_part + reduce_pieces(mlp_part, "mlp", n_mlp))
    result = jnp.concatenate(outs, axis=0)
    share_ids = share_start + jnp.arange(share_rows)
    valid = share_ids < lengths[0]
    return jnp.where(valid[:, None], result, jnp.float32(0.0)).astype(jnp.bfloat16)


def solution(mesh):
    return jax.shard_map(
        shards,
        mesh=mesh,
        in_specs=(
            P("req", "mlp", None),
            P(),
            P("mlp", None),
            P("req"),
            P("req"),
            P("req", None),
            P(),
            P(None, "mlp"),
            P("mlp", None),
            P(),
            P("req", "mlp"),
            P("mlp", "req"),
        ),
        out_specs=P(("req", "mlp"), None),
        check_vma=False,
    )
```

```python
import jax
import jax.numpy as jnp
from jax import lax
from jax.sharding import PartitionSpec as P

HD = 104
MLP_CHUNKS = 2
TAG = 128


def rms_scale(values, gain):
    wide = values.astype(jnp.float32)
    power = jnp.mean(wide * wide, axis=-1, keepdims=True)
    return wide * lax.rsqrt(power + 1e-06) * gain


def reduce_pieces(part, axis, count):
    pieces = lax.all_to_all(part.reshape((count, -1) + part.shape[1:]), axis, 0, 0, tiled=True)
    return jnp.sum(pieces.astype(jnp.float32), axis=0)


def gather_pieces(share, axis, count):
    spread = jnp.broadcast_to(share[None], (count,) + share.shape)
    return lax.all_to_all(spread, axis, 0, 0, tiled=True).reshape((-1,) + share.shape[1:])


def shards(
    patches, vis_gain, vis_proj, targets, lengths, text, attn_gain, wqkv, wo, mlp_gain, w_in, w_out
):
    requests = lax.axis_size("req")
    n_mlp = lax.axis_size("mlp")
    group = lax.axis_index("mlp")
    me = lax.axis_index("req")
    seq_len = text.shape[0]
    width = text.shape[1]
    merged_count = patches.shape[0]
    capacity = 2 * merged_count // requests

    in_rows = w_in.shape[0]
    hidden = w_in.shape[1]
    in_blocks = lax.all_gather(w_in, "req", axis=0)

    patch_norm = rms_scale(patches[:, 0, :], vis_gain).astype(jnp.bfloat16)
    partial_value = jnp.dot(patch_norm, vis_proj, preferred_element_type=jnp.float32)
    vis_mine = reduce_pieces(partial_value.astype(jnp.bfloat16), "mlp", n_mlp).astype(jnp.bfloat16)
    image_rows = gather_pieces(vis_mine, "mlp", n_mlp)

    target_req = targets // seq_len
    position = targets % seq_len
    tag = jnp.stack(
        [position // 32, position % 32, jnp.ones_like(position)], axis=1
    ).astype(jnp.bfloat16)
    tagged = jnp.concatenate([image_rows, jnp.pad(tag, ((0, 0), (0, TAG - 3)))], axis=1)
    one_hot = (target_req[:, None] == jnp.arange(requests)[None, :]).astype(jnp.int32)
    before = jnp.cumsum(one_hot, axis=0) - one_hot
    rank_in = jnp.sum(before * one_hot, axis=1)
    slot_ids = target_req * capacity + rank_in
    buffer = jnp.zeros((requests * capacity, width + TAG), jnp.bfloat16).at[slot_ids].set(tagged)
    buffer = buffer.reshape(requests, capacity, width + TAG)
    received = lax.all_to_all(buffer, "req", split_axis=0, concat_axis=0, tiled=True)
    received, w_in_full, out_local = lax.optimization_barrier(
        (received, in_blocks.reshape(-1, hidden), w_out.T)
    )
    out_blocks = lax.all_gather(out_local, "req", axis=0)
    arrived = received.reshape(requests * capacity, width + TAG)
    got = arrived[:, width : width + 3].astype(jnp.int32)
    flat_slots = jnp.where(got[:, 2] > 0, got[:, 0] * 32 + got[:, 1], seq_len)
    arrivals = requests * capacity
    source_of = (
        jnp.full((seq_len,), arrivals, jnp.int32)
        .at[flat_slots]
        .set(jnp.arange(arrivals, dtype=jnp.int32), mode="drop")
    )
    picked = jnp.take(arrived[:, :width], jnp.minimum(source_of, arrivals - 1), axis=0)
    embedded = jnp.where((source_of < arrivals)[:, None], picked, text)

    attn_in = rms_scale(embedded, attn_gain).astype(jnp.bfloat16)
    qkv = jnp.dot(attn_in, wqkv, preferred_element_type=jnp.float32).astype(jnp.bfloat16)
    local_heads = wqkv.shape[1] // (3 * HD)
    qkv = qkv.reshape(seq_len, local_heads, 3, HD)
    query, keys, values = (qkv[:, :, 0], qkv[:, :, 1], qkv[:, :, 2])
    scores = (
        jnp.einsum("qhd,khd->hqk", query, keys, preferred_element_type=jnp.float32)
        / jnp.float32(HD) ** 0.5
    )
    share_rows = seq_len // n_mlp
    share_start = group * share_rows
    sub = share_rows // MLP_CHUNKS
    scale = jnp.float32(HD) ** 0.5
    row_ids = jnp.arange(seq_len).reshape(n_mlp, share_rows)
    key_ids = jnp.arange(seq_len)
    q_split = query.reshape(n_mlp, share_rows, local_heads, HD)
    embedded_share = lax.dynamic_slice_in_dim(embedded, share_start, share_rows, 0)
    resids, gathered = [], []
    for chunk in range(MLP_CHUNKS):
        q_rows = q_split[:, chunk * sub : (chunk + 1) * sub].reshape(n_mlp * sub, local_heads, HD)
        q_ids = row_ids[:, chunk * sub : (chunk + 1) * sub].reshape(-1)
        scores = (
            jnp.einsum("qhd,khd->hqk", q_rows, keys, preferred_element_type=jnp.float32) / scale
        )
        causal = key_ids[None, :] <= q_ids[:, None]
        scores = jnp.where(causal[None], scores, jnp.float32(-1e30))
        peak = jnp.max(scores, axis=-1, keepdims=True)
        weights = jnp.exp(scores - peak)
        probs = (weights / jnp.sum(weights, axis=-1, keepdims=True)).astype(jnp.bfloat16)
        context = jnp.einsum(
            "hqk,khd->qhd", probs, values, preferred_element_type=jnp.float32
        ).astype(jnp.bfloat16)
        context = context.reshape(n_mlp * sub, local_heads * HD)
        attn_part = jnp.dot(context, wo, preferred_element_type=jnp.float32).astype(jnp.bfloat16)
        attn_pieces = lax.all_to_all(
            attn_part.reshape(n_mlp, sub, width), "mlp", 0, 0, tiled=True
        )
        if chunk == MLP_CHUNKS - 1:
            attn_pieces, w_out_t = lax.optimization_barrier(
                (attn_pieces, out_blocks.reshape(-1, hidden))
            )
        resid_part = embedded_share[chunk * sub : (chunk + 1) * sub].astype(jnp.float32) + jnp.sum(
            attn_pieces.astype(jnp.float32), axis=0
        )
        mlp_in_part = rms_scale(resid_part, mlp_gain).astype(jnp.bfloat16)
        resids.append(resid_part)
        if chunk == 0:
            gathered.append(lax.all_gather(mlp_in_part, "mlp", axis=0, tiled=True))
        else:
            gathered.append(gather_pieces(mlp_in_part, "mlp", n_mlp))
    outs = []
    for resid_part, rows_in in zip(resids, gathered):
        upward = jnp.dot(rows_in, w_in_full, preferred_element_type=jnp.float32)
        active = jax.nn.gelu(upward, approximate=False).astype(jnp.bfloat16)
        mlp_part = lax.dot_general(
            active, w_out_t, (((1,), (1,)), ((), ())), preferred_element_type=jnp.float32
        ).astype(jnp.bfloat16)
        outs.append(resid_part + reduce_pieces(mlp_part, "mlp", n_mlp))
    result = jnp.concatenate(outs, axis=0)
    share_ids = share_start + jnp.arange(share_rows)
    valid = share_ids < lengths[0]
    return jnp.where(valid[:, None], result, jnp.float32(0.0)).astype(jnp.bfloat16)


def solution(mesh):
    return jax.shard_map(
        shards,
        mesh=mesh,
        in_specs=(
            P("req", "mlp", None),
            P(),
            P("mlp", None),
            P("req"),
            P("req"),
            P("req", None),
            P(),
            P(None, "mlp"),
            P("mlp", None),
            P(),
            P("req", "mlp"),
            P("mlp", "req"),
        ),
        out_specs=P(("req", "mlp"), None),
        check_vma=False,
    )
```
